1024 devices in a mesh: ctx: 64 (over x, z), head: 16 (over y, core).
Axes of the slice: x: 8, y: 8, z: 8, core: 2. Of those that a mesh axis runs over, the one named last changes fastest.
Arguments:
- queries: bfloat16 [24576, 8192], P('ctx', 'head'), may hold values from -6 to 6
- keys: bfloat16 [24576, 8192], P('ctx', 'head'), may hold values from -6 to 6
- values: bfloat16 [24576, 8192], P('ctx', 'head'), may hold values from -6 to 6
- doc_lengths: int32 [128], replicated, may hold values from 1 to 1536, 24576 in all
- norm_gain: float32 [8192], P('head'), may hold values from 0.5 to 1.5
- w_out: bfloat16 [8192, 6144], P('head'), may hold values from -0.0625 to 0.0625
Outputs:
- layer_out: bfloat16 [24576, 6144], P(('ctx', 'head'))
The draws below stay inside these ranges and needn't reach their ends.
Inputs may be any that keep to these rules, and one draw needn't show every extreme that they name: `doc_lengths`: positive lengths of the 128 documents in order, summing to 24576; the longest has exactly 1536 tokens.
All inputs are finite; a program needn't handle non-finite values.
Results may differ from the reference program's by a relative error of at most 0.019.
Values may be sent and summed in bfloat16 or wider, within the bound.
No kernel may reach another device: no remote copies, remote signals or barrier semaphores. Data moves between devices by JAX's collectives and lax.ppermute only.
A program may use at most 64 MiB of HBM per device.

```python
import math
import jax
import jax.numpy as jnp
import numpy as np
from jax import lax

HEADS = 64
DH = 128
DM = 6144
TOK_DEV = 384
TOKENS = 24576
MAXDOC = 1536
NDOCS = 128
N_HEAD = 16


def block_scale(key, extent, cuts, least, top_value):
    level, own = 1.0, jax.random.fold_in(key, 6)
    for dim, blocks in cuts:
        steps = jnp.exp(jax.random.uniform(jax.random.fold_in(own, dim), (blocks,), jnp.float32, least / len(cuts), top_value / len(cuts)))
        level = level * jnp.repeat(steps, extent[dim] // blocks).reshape([-1 if axis == dim else 1 for axis in range(len(extent))])
    return level


def profile(amount, total, bound, skew):
    weights = [(1 << 20) // math.isqrt(standing ** skew) + 1 for standing in range(2, amount + 1)]
    spare, given = total - bound - (amount - 1), [1] * (amount - 1)
    while spare > 0:
        movable = [i for i in range(amount - 1) if given[i] < bound]
        whole, remaining = sum([weights[i] for i in movable]), spare
        for i in movable:
            extra = min(bound - given[i], max(1, remaining * weights[i] // whole), spare)
            given[i] = given[i] + extra
            spare = spare - extra
    return np.array([bound] + given)


def ragged_sizes(own_key, amount, total, bound, lean):
    if amount == 2:
        one = jax.random.randint(own_key, (), max(1, total - bound), min(bound, total - 1) + 1)
        return jnp.stack([one, total - one])
    lengths = jnp.asarray(profile(amount, total, bound, lean), jnp.int32)
    pairs = (amount - 1) // 2
    source_of, receiver = lengths[1:1 + 2 * pairs:2], lengths[2:2 + 2 * pairs:2]
    room = jnp.minimum(source_of - 1, bound - receiver)
    moved = jax.random.randint(jax.random.fold_in(own_key, 1), (pairs,), 0, 1 << 20) % (room + 1)
    lengths = lengths.at[1:1 + 2 * pairs:2].set(source_of - moved).at[2:2 + 2 * pairs:2].set(receiver + moved)
    return lengths[jax.random.permutation(jax.random.fold_in(own_key, 2), amount)]


def bell_draw(rng, extent, deviation, bound, shards=(), kind=jnp.bfloat16):
    entries = deviation * jax.random.normal(rng, extent, jnp.float32)
    if shards:
        entries = entries * block_scale(rng, extent, shards, -0.22, 0.18)
    return jnp.clip(entries, -bound, bound).astype(kind)


def setup_inputs(seed: int = 0) -> dict:
    streams_of = jax.random.split(jax.random.key(seed), 7)
    queries = bell_draw(streams_of[0], (TOKENS, HEADS * DH), 1.0, 6.0, ((0, 64), (1, 16)))
    keys = bell_draw(streams_of[1], (TOKENS, HEADS * DH), 1.0, 6.0, ((0, 64), (1, 16)))
    values = bell_draw(streams_of[2], (TOKENS, HEADS * DH), 1.0, 6.0, ((0, 64), (1, 16)))
    doc_lengths = ragged_sizes(streams_of[3], NDOCS, TOKENS, MAXDOC, 2).astype(jnp.int32)
    norm_gain = jnp.clip(1.0 + 0.1 * jax.random.normal(streams_of[4], (HEADS * DH,), jnp.float32), 0.5, 1.5)
    w_out = bell_draw(streams_of[5], (HEADS * DH, DM), (HEADS * DH) ** -0.5, 0.0625, ((0, 16),))
    return {"queries": queries, "keys": keys, "values": values, "doc_lengths": doc_lengths, "norm_gain": norm_gain, "w_out": w_out}


def reference(queries, keys, values, doc_lengths, norm_gain, w_out):
    ends = jnp.cumsum(doc_lengths).astype(jnp.int32)
    blocks = TOKENS // TOK_DEV
    q_all = queries.reshape(blocks, TOK_DEV, HEADS, DH)
    k_all = keys.reshape(blocks, TOK_DEV, HEADS, DH)
    v_all = values.reshape(blocks, TOK_DEV, HEADS, DH)
    offsets = jnp.arange(TOK_DEV, dtype=jnp.int32)
    causal = offsets[:, None] >= offsets[None, :]

    def advance(carry, inputs):
        state, open_doc = carry
        q_blk, k_blk, v_blk, index = inputs
        where_now = (index * TOK_DEV + offsets).astype(jnp.int32)
        doc = lax.optimization_barrier(jnp.sum((ends[None, :] <= where_now[:, None]).astype(jnp.int32), axis=1)).astype(jnp.int32)
        scores = jnp.einsum('thd,shd->hts', q_blk.astype(jnp.float32), k_blk.astype(jnp.float32))
        allowed = (doc[:, None] == doc[None, :]) & causal
        weights = jnp.where(allowed[None], scores, 0.0).astype(jnp.bfloat16)
        intra = jnp.einsum('hts,shd->thd', weights.astype(jnp.float32), v_blk.astype(jnp.float32))
        active = (doc == open_doc).astype(jnp.float32)
        inter = jnp.einsum('thd,hde->the', q_blk.astype(jnp.float32), state, precision=lax.Precision.HIGHEST)
        inter = inter * active[:, None, None]
        last = doc == doc[-1]
        k_last = jnp.where(last[:, None, None], k_blk, jnp.zeros_like(k_blk)).astype(jnp.float32)
        block_state = jnp.einsum('thd,the->hde', k_last, v_blk.astype(jnp.float32))
        new_state = jnp.where(doc[-1] == open_doc, state + block_state, block_state)
        return ((new_state, doc[-1].astype(jnp.int32)), intra + inter)
    start = (jnp.zeros((HEADS, DH, DH), jnp.float32), jnp.array(-1, jnp.int32))
    _, attn = lax.scan(advance, start, (q_all, k_all, v_all, jnp.arange(blocks, dtype=jnp.int32)))
    attn = attn.reshape(TOKENS, HEADS, DH)
    meansq = lax.optimization_barrier(jnp.mean(attn * attn, axis=-1, keepdims=True))
    normed = attn * lax.rsqrt(meansq + 1e-06) * norm_gain.reshape(HEADS, DH)
    hidden = normed.reshape(TOKENS, HEADS * DH).astype(jnp.bfloat16)
    group_rows = HEADS * DH // N_HEAD
    hidden_groups = hidden.reshape(TOKENS, N_HEAD, group_rows).transpose(1, 0, 2)
    weight_groups = w_out.reshape(N_HEAD, group_rows, DM)

    def add_group(total, pair):
        piece, weight = pair
        partial_out = jnp.dot(piece, weight, preferred_element_type=jnp.float32).astype(jnp.bfloat16)
        return (total + partial_out.astype(jnp.float32), None)
    total, _ = lax.scan(add_group, jnp.zeros((TOKENS, DM), jnp.float32), (hidden_groups, weight_groups))
    return total.astype(jnp.bfloat16)
```

```python
import jax
import jax.numpy as jnp
from jax import lax
from jax.sharding import PartitionSpec as P

DH = 128


def shift_from(x, axis, size, step):
    return lax.ppermute(x, axis, [(i, i + step) for i in range(size - step)])


def local(n_ctx, n_head, queries, keys, values, doc_lengths, norm_gain, w_out):
    tok = queries.shape[0]
    heads_here = queries.shape[1] // DH
    place = lax.axis_index("ctx")
    first = place * tok
    ends = jnp.cumsum(doc_lengths)

    def doc_at(p):
        return jnp.sum((ends <= p).astype(jnp.int32))

    def whole_open(j):
        return ((j > 0) & (doc_at(j * tok - 1) == doc_at(j * tok + tok - 1))).astype(jnp.float32)

    offsets = jnp.arange(tok, dtype=jnp.int32)
    where_now = first + offsets
    doc = jnp.sum((ends[None, :] <= where_now[:, None]).astype(jnp.int32), axis=1)
    continues = (place > 0) & (doc_at(first - 1) == doc[0])
    q_heads = queries.reshape(tok, heads_here, DH)
    k_heads = keys.reshape(tok, heads_here, DH)
    v_heads = values.reshape(tok, heads_here, DH)

    last = doc == doc[-1]
    k_last = jnp.where(last[:, None, None], k_heads, jnp.zeros_like(k_heads))
    own = jnp.einsum("thd,the->hde", k_last, v_heads, preferred_element_type=jnp.float32)
    wo0 = whole_open(place)
    wo1 = whole_open(place - 1)
    r1 = shift_from(own.astype(jnp.bfloat16), "ctx", n_ctx, 1).astype(jnp.float32)
    t1 = own + wo0 * r1
    r2 = shift_from(t1.astype(jnp.bfloat16), "ctx", n_ctx, 2).astype(jnp.float32)
    t2 = t1 + (wo0 * wo1) * r2
    r3 = shift_from(t2.astype(jnp.bfloat16), "ctx", n_ctx, 1).astype(jnp.float32)
    carried = r3 * continues.astype(jnp.float32)

    causal = offsets[:, None] >= offsets[None, :]
    allowed = (doc[:, None] == doc[None, :]) & causal
    scores = jnp.einsum("thd,shd->hts", q_heads, k_heads, preferred_element_type=jnp.float32)
    weights = jnp.where(allowed[None], scores, 0.0).astype(jnp.bfloat16)
    intra = jnp.einsum("hts,shd->thd", weights, v_heads, preferred_element_type=jnp.float32)
    active = (continues & (doc == doc[0])).astype(jnp.float32)
    inter = jnp.einsum(
        "thd,hde->the", q_heads.astype(jnp.float32), carried, precision=lax.Precision.HIGHEST
    )
    attn = intra + inter * active[:, None, None]
    meansq = jnp.mean(attn * attn, axis=-1, keepdims=True)
    normed = attn * lax.rsqrt(meansq + 1e-06) * norm_gain.reshape(heads_here, DH)
    hidden = normed.reshape(tok, heads_here * DH).astype(jnp.bfloat16)

    n_chip = n_head // 2
    rows = tok // n_head
    me = lax.axis_index("head")
    core = me % 2
    chip = me // 2
    by_owner = hidden.reshape(n_chip, 2, rows, hidden.shape[1])
    mine_rows = lax.dynamic_index_in_dim(by_owner, core, 1, False).reshape(n_chip * rows, -1)
    other_rows = lax.dynamic_index_in_dim(by_owner, 1 - core, 1, False).reshape(n_chip * rows, -1)
    other_part = jnp.dot(other_rows, w_out, preferred_element_type=jnp.float32).astype(jnp.bfloat16)
    sibling = lax.ppermute(other_part, "head", [(i, i ^ 1) for i in range(n_head)])
    mine_part = jnp.dot(mine_rows, w_out, preferred_element_type=jnp.float32).astype(jnp.bfloat16)
    acc = (mine_part.astype(jnp.float32) + sibling.astype(jnp.float32)).reshape(n_chip, rows, -1)

    width = acc.shape[2] // 2
    cw_own = acc[:, :, :width]
    ccw_own = acc[:, :, width:]
    cw_perm = [(i, (i + 2) % n_head) for i in range(n_head)]
    ccw_perm = [(i, (i - 2) % n_head) for i in range(n_head)]

    def chunk(a, idx):
        return lax.dynamic_index_in_dim(a, idx % n_chip, 0, False)

    cw_send = chunk(cw_own, chip - 1)
    ccw_send = chunk(ccw_own, chip + 1)
    for s in range(n_chip - 1):
        cw_recv = lax.ppermute(cw_send.astype(jnp.bfloat16), "head", cw_perm).astype(jnp.float32)
        ccw_recv = lax.ppermute(ccw_send.astype(jnp.bfloat16), "head", ccw_perm).astype(jnp.float32)
        cw_send = cw_recv + chunk(cw_own, chip - s - 2)
        ccw_send = ccw_recv + chunk(ccw_own, chip + s + 2)
    return jnp.concatenate([cw_send, ccw_send], axis=1).astype(jnp.bfloat16)


def solution(mesh):
    placed = (P("ctx", "head"), P("ctx", "head"), P("ctx", "head"), P(), P("head"), P("head", None))
    n_ctx, n_head = mesh.shape["ctx"], mesh.shape["head"]
    return jax.shard_map(
        lambda *a: local(n_ctx, n_head, *a),
        mesh=mesh,
        in_specs=placed,
        out_specs=P(("ctx", "head"), None),
        check_vma=False,
    )
```

```python
import jax
import jax.numpy as jnp
from jax import lax
from jax.sharding import PartitionSpec as P

DH = 128


def shift_from(x, axis, size, step):
    return lax.ppermute(x, axis, [(i, i + step) for i in range(size - step)])


def local(n_ctx, n_head, queries, keys, values, doc_lengths, norm_gain, w_out):
    tok = queries.shape[0]
    heads_here = queries.shape[1] // DH
    place = lax.axis_index("ctx")
    first = place * tok
    ends = jnp.cumsum(doc_lengths)

    def doc_at(p):
        return jnp.sum((ends <= p).astype(jnp.int32))

    def whole_open(j):
        return ((j > 0) & (doc_at(j * tok - 1) == doc_at(j * tok + tok - 1))).astype(jnp.float32)

    offsets = jnp.arange(tok, dtype=jnp.int32)
    where_now = first + offsets
    doc = jnp.sum((ends[None, :] <= where_now[:, None]).astype(jnp.int32), axis=1)
    continues = (place > 0) & (doc_at(first - 1) == doc[0])
    q_heads = queries.reshape(tok, heads_here, DH)
    k_heads = keys.reshape(tok, heads_here, DH)
    v_heads = values.reshape(tok, heads_here, DH)

    last = doc == doc[-1]
    k_last = jnp.where(last[:, None, None], k_heads, jnp.zeros_like(k_heads))
    own = jnp.einsum("thd,the->hde", k_last, v_heads, preferred_element_type=jnp.float32)
    wo0 = whole_open(place)
    wo1 = whole_open(place - 1)
    wo2 = whole_open(place - 2)
    own_b = own.astype(jnp.bfloat16)
    r1 = shift_from(own_b, "ctx", n_ctx, 1).astype(jnp.float32)
    r2 = shift_from(own_b, "ctx", n_ctx, 2).astype(jnp.float32)
    pair = own + wo0 * r1
    r3 = shift_from(pair.astype(jnp.bfloat16), "ctx", n_ctx, 3).astype(jnp.float32)
    carried = (r1 + wo1 * (r2 + wo2 * r3)) * continues.astype(jnp.float32)

    causal = offsets[:, None] >= offsets[None, :]
    allowed = (doc[:, None] == doc[None, :]) & causal
    scores = jnp.einsum("thd,shd->hts", q_heads, k_heads, preferred_element_type=jnp.float32)
    weights = jnp.where(allowed[None], scores, 0.0).astype(jnp.bfloat16)
    intra = jnp.einsum("hts,shd->thd", weights, v_heads, preferred_element_type=jnp.float32)
    active = (continues & (doc == doc[0])).astype(jnp.float32)
    inter = jnp.einsum(
        "thd,hde->the", q_heads.astype(jnp.float32), carried, precision=lax.Precision.HIGHEST
    )
    attn = intra + inter * active[:, None, None]
    meansq = jnp.mean(attn * attn, axis=-1, keepdims=True)
    normed = attn * lax.rsqrt(meansq + 1e-06) * norm_gain.reshape(heads_here, DH)
    hidden = normed.reshape(tok, heads_here * DH).astype(jnp.bfloat16)

    n_chip = n_head // 2
    rows = tok // n_head
    me = lax.axis_index("head")
    core = me % 2
    chip = me // 2
    by_owner = hidden.reshape(n_chip, 2, rows, hidden.shape[1])
    mine_rows = lax.dynamic_index_in_dim(by_owner, core, 1, False).reshape(n_chip * rows, -1)
    other_rows = lax.dynamic_index_in_dim(by_owner, 1 - core, 1, False).reshape(n_chip * rows, -1)
    other_part = jnp.dot(other_rows, w_out, preferred_element_type=jnp.float32).astype(jnp.bfloat16)
    sibling = lax.ppermute(other_part, "head", [(i, i ^ 1) for i in range(n_head)])
    mine_part = lax.optimization_barrier(
        jnp.dot(mine_rows, w_out, preferred_element_type=jnp.float32).astype(jnp.bfloat16)
    )
    acc = (mine_part.astype(jnp.float32) + sibling.astype(jnp.float32)).reshape(n_chip, rows, -1)

    cw_perm = [(i, (i + 2) % n_head) for i in range(n_head)]
    ccw_perm = [(i, (i - 2) % n_head) for i in range(n_head)]

    def chunk(idx):
        return lax.dynamic_index_in_dim(acc, idx % n_chip, 0, False)

    cw_steps = n_chip // 2
    ccw_steps = n_chip - 1 - cw_steps
    cw_send = chunk(chip + cw_steps)
    ccw_send = chunk(chip - ccw_steps)
    for s in range(cw_steps):
        cw_recv = lax.ppermute(cw_send.astype(jnp.bfloat16), "head", cw_perm).astype(jnp.float32)
        if s < ccw_steps:
            ccw_recv = lax.ppermute(ccw_send.astype(jnp.bfloat16), "head", ccw_perm).astype(jnp.float32)
        if s < cw_steps - 1:
            cw_send = cw_recv + chunk(chip + cw_steps - 1 - s)
        if s < ccw_steps - 1:
            ccw_send = ccw_recv + chunk(chip - ccw_steps + 1 + s)
    return (cw_recv + ccw_recv + chunk(chip)).astype(jnp.bfloat16)


def solution(mesh):
    placed = (P("ctx", "head"), P("ctx", "head"), P("ctx", "head"), P(), P("head"), P("head", None))
    n_ctx, n_head = mesh.shape["ctx"], mesh.shape["head"]
    return jax.shard_map(
        lambda *a: local(n_ctx, n_head, *a),
        mesh=mesh,
        in_specs=placed,
        out_specs=P(("ctx", "head"), None),
        check_vma=False,
    )
```

```python
import jax
import jax.numpy as jnp
from jax import lax
from jax.sharding import PartitionSpec as P

DH = 128


def shift_from(x, axis, size, step):
    return lax.ppermute(x, axis, [(i, i + step) for i in range(size - step)])


def local(n_ctx, n_head, queries, keys, values, doc_lengths, norm_gain, w_out):
    tok = queries.shape[0]
    heads_here = queries.shape[1] // DH
    place = lax.axis_index("ctx")
    first = place * tok
    ends = jnp.cumsum(doc_lengths)

    def doc_at(p):
        return jnp.sum((ends <= p).astype(jnp.int32))

    def whole_open(j):
        return ((j > 0) & (doc_at(j * tok - 1) == doc_at(j * tok + tok - 1))).astype(jnp.float32)

    offsets = jnp.arange(tok, dtype=jnp.int32)
    where_now = first + offsets
    doc = jnp.sum((ends[None, :] <= where_now[:, None]).astype(jnp.int32), axis=1)
    continues = (place > 0) & (doc_at(first - 1) == doc[0])
    q_heads = queries.reshape(tok, heads_here, DH)
    k_heads = keys.reshape(tok, heads_here, DH)
    v_heads = values.reshape(tok, heads_here, DH)

    last = doc == doc[-1]
    k_last = jnp.where(last[:, None, None], k_heads, jnp.zeros_like(k_heads))
    own = jnp.einsum("thd,the->hde", k_last, v_heads, preferred_element_type=jnp.float32)
    wo0 = whole_open(place)
    wo1 = whole_open(place - 1)
    wo2 = whole_open(place - 2)
    own_b = own.astype(jnp.bfloat16)
    r1 = shift_from(own_b, "ctx", n_ctx, 1).astype(jnp.float32)
    r2 = shift_from(own_b, "ctx", n_ctx, 2).astype(jnp.float32)
    pair = own + wo0 * r1
    r3 = shift_from(pair.astype(jnp.bfloat16), "ctx", n_ctx, 3).astype(jnp.float32)
    carried = (r1 + wo1 * (r2 + wo2 * r3)) * continues.astype(jnp.float32)

    causal = offsets[:, None] >= offsets[None, :]
    allowed = (doc[:, None] == doc[None, :]) & causal
    scores = jnp.einsum("thd,shd->hts", q_heads, k_heads, preferred_element_type=jnp.float32)
    weights = jnp.where(allowed[None], scores, 0.0).astype(jnp.bfloat16)
    intra = jnp.einsum("hts,shd->thd", weights, v_heads, preferred_element_type=jnp.float32)
    active = (continues & (doc == doc[0])).astype(jnp.float32)
    inter = jnp.einsum(
        "thd,hde->the", q_heads.astype(jnp.float32), carried, precision=lax.Precision.HIGHEST
    )
    attn = intra + inter * active[:, None, None]
    meansq = jnp.mean(attn * attn, axis=-1, keepdims=True)
    normed = attn * lax.rsqrt(meansq + 1e-06) * norm_gain.reshape(heads_here, DH)
    hidden = normed.reshape(tok, heads_here * DH).astype(jnp.bfloat16)

    n_chip = n_head // 2
    rows = tok // n_head
    me = lax.axis_index("head")
    core = me % 2
    chip = me // 2
    by_owner = hidden.reshape(n_chip, 2, rows, hidden.shape[1])
    mine_rows = lax.dynamic_index_in_dim(by_owner, core, 1, False).reshape(n_chip * rows, -1)
    other_rows = lax.dynamic_index_in_dim(by_owner, 1 - core, 1, False).reshape(n_chip * rows, -1)
    other_part = jnp.dot(other_rows, w_out, preferred_element_type=jnp.float32).astype(jnp.bfloat16)
    sibling = lax.ppermute(other_part, "head", [(i, i ^ 1) for i in range(n_head)])
    mine_part = lax.optimization_barrier(
        jnp.dot(mine_rows, w_out, preferred_element_type=jnp.float32).astype(jnp.bfloat16)
    )
    mine_part = mine_part.reshape(n_chip, rows, -1)
    sibling = sibling.reshape(n_chip, rows, -1)
    width = mine_part.shape[2] // 2

    cw_perm = [(i, (i + 2) % n_head) for i in range(n_head)]
    ccw_perm = [(i, (i - 2) % n_head) for i in range(n_head)]

    def chunk(idx):
        idx = idx % n_chip
        a = lax.dynamic_index_in_dim(mine_part, idx, 0, False).astype(jnp.float32)
        return a + lax.dynamic_index_in_dim(sibling, idx, 0, False).astype(jnp.float32)

    def send(x, perm):
        return lax.ppermute(x.astype(jnp.bfloat16), "head", perm).astype(jnp.float32)

    half = n_chip // 2
    cw_recv = send(chunk(chip + half)[:, :width], cw_perm)
    ccw_recv = send(chunk(chip - half)[:, width:], ccw_perm)
    for s in range(half - 1):
        cw_own = chunk(chip + half - 1 - s)
        ccw_own = chunk(chip - half + 1 + s)
        if s == 0:
            cw_own = jnp.concatenate([cw_own[:, :width] + cw_recv, cw_own[:, width:]], axis=1)
            ccw_own = jnp.concatenate([ccw_own[:, :width], ccw_own[:, width:] + ccw_recv], axis=1)
        else:
            cw_own = cw_own + cw_recv
            ccw_own = ccw_own + ccw_recv
        cw_recv = send(cw_own, cw_perm)
        ccw_recv = send(ccw_own, ccw_perm)
    return (cw_recv + ccw_recv + chunk(chip)).astype(jnp.bfloat16)


def solution(mesh):
    placed = (P("ctx", "head"), P("ctx", "head"), P("ctx", "head"), P(), P("head"), P("head", None))
    n_ctx, n_head = mesh.shape["ctx"], mesh.shape["head"]
    return jax.shard_map(
        lambda *a: local(n_ctx, n_head, *a),
        mesh=mesh,
        in_specs=placed,
        out_specs=P(("ctx", "head"), None),
        check_vma=False,
    )
```

```python
import jax
import jax.numpy as jnp
from jax import lax
from jax.sharding import PartitionSpec as P

DH = 128


def shift_from(x, axis, size, step):
    return lax.ppermute(x, axis, [(i, i + step) for i in range(size - step)])


def local(n_ctx, n_head, queries, keys, values, doc_lengths, norm_gain, w_out):
    tok = queries.shape[0]
    heads_here = queries.shape[1] // DH
    place = lax.axis_index("ctx")
    first = place * tok
    ends = jnp.cumsum(doc_lengths)

    def doc_at(p):
        return jnp.sum((ends <= p).astype(jnp.int32))

    def whole_open(j):
        return ((j > 0) & (doc_at(j * tok - 1) == doc_at(j * tok + tok - 1))).astype(jnp.float32)

    offsets = jnp.arange(tok, dtype=jnp.int32)
    where_now = first + offsets
    doc = jnp.sum((ends[None, :] <= where_now[:, None]).astype(jnp.int32), axis=1)
    continues = (place > 0) & (doc_at(first - 1) == doc[0])
    q_heads = queries.reshape(tok, heads_here, DH)
    k_heads = keys.reshape(tok, heads_here, DH)
    v_heads = values.reshape(tok, heads_here, DH)

    last = doc == doc[-1]
    k_last = jnp.where(last[:, None, None], k_heads, jnp.zeros_like(k_heads))
    own = jnp.einsum("thd,the->hde", k_last, v_heads, preferred_element_type=jnp.float32)
    wo0 = whole_open(place)
    wo1 = whole_open(place - 1)
    wo2 = whole_open(place - 2)
    own_b = own.astype(jnp.bfloat16)
    r1 = shift_from(own_b, "ctx", n_ctx, 1).astype(jnp.float32)
    r2 = shift_from(own_b, "ctx", n_ctx, 2).astype(jnp.float32)
    pair = own + wo0 * r1
    r3 = shift_from(pair.astype(jnp.bfloat16), "ctx", n_ctx, 3).astype(jnp.float32)
    carried = (r1 + wo1 * (r2 + wo2 * r3)) * continues.astype(jnp.float32)

    causal = offsets[:, None] >= offsets[None, :]
    allowed = (doc[:, None] == doc[None, :]) & causal
    scores = jnp.einsum("thd,shd->hts", q_heads, k_heads, preferred_element_type=jnp.float32)
    weights = jnp.where(allowed[None], scores, 0.0).astype(jnp.bfloat16)
    intra = jnp.einsum("hts,shd->thd", weights, v_heads, preferred_element_type=jnp.float32)
    active = (continues & (doc == doc[0])).astype(jnp.float32)
    inter = jnp.einsum(
        "thd,hde->the", q_heads.astype(jnp.float32), carried, precision=lax.Precision.HIGHEST
    )
    attn = intra + inter * active[:, None, None]
    meansq = jnp.mean(attn * attn, axis=-1, keepdims=True)
    normed = attn * lax.rsqrt(meansq + 1e-06) * norm_gain.reshape(heads_here, DH)
    hidden = normed.reshape(tok, heads_here * DH).astype(jnp.bfloat16)

    n_chip = n_head // 2
    rows = tok // n_chip
    half_rows = rows // 2
    me = lax.axis_index("head")
    core = me % 2
    chip = me // 2
    dirn = 1 - 2 * core
    width = w_out.shape[1] // 2
    by_chip = hidden.reshape(n_chip, rows, hidden.shape[1])

    def take(a, idx):
        return lax.dynamic_index_in_dim(a, idx % n_chip, 0, False)

    def halves(a, which):
        return lax.dynamic_slice_in_dim(a, which * half_rows, half_rows, 0)

    def cols(a, which):
        return lax.dynamic_slice_in_dim(a, which * width, width, 1)

    far = chip + n_chip // 2
    steps = n_chip // 2 - 1
    sib_rows = jnp.concatenate(
        [take(by_chip, chip - dirn * j) for j in range(1, steps + 1)]
        + [take(by_chip, far), halves(take(by_chip, chip), 1 - core)],
        axis=0,
    )
    sib_part = jnp.dot(sib_rows, w_out, preferred_element_type=jnp.float32).astype(jnp.bfloat16)
    far_part = sib_part[steps * rows:(steps + 1) * rows]
    to_sib = jnp.concatenate(
        [
            sib_part[:steps * rows],
            cols(far_part, 1 - core).reshape(half_rows, -1),
            sib_part[(steps + 1) * rows:],
        ],
        axis=0,
    )
    from_sib = lax.ppermute(to_sib, "head", [(i, i ^ 1) for i in range(n_head)]).astype(jnp.float32)
    my_rows = jnp.concatenate(
        [take(by_chip, chip + dirn * j) for j in range(1, steps + 1)]
        + [halves(take(by_chip, chip), core)],
        axis=0,
    )
    my_part = lax.optimization_barrier(
        jnp.dot(my_rows, w_out, preferred_element_type=jnp.float32).astype(jnp.bfloat16)
    ).astype(jnp.float32)

    def near(j):
        return my_part[(j - 1) * rows:j * rows] + from_sib[(j - 1) * rows:j * rows]

    far_sum = cols(far_part, core).astype(jnp.float32) + from_sib[
        steps * rows:steps * rows + half_rows
    ].reshape(rows, width)
    own_sum = my_part[steps * rows:] + from_sib[steps * rows + half_rows:]

    ring = [(i, (i + 2) % n_head) if i % 2 == 0 else (i, (i - 2) % n_head) for i in range(n_head)]

    def send(x, perm):
        return lax.ppermute(x.astype(jnp.bfloat16), "head", perm).astype(jnp.float32)

    recv = send(far_sum, ring)
    zeros = jnp.zeros((rows, width), jnp.float32)
    for j in range(steps, 0, -1):
        if j == steps:
            lead = jnp.where(core == 0, jnp.concatenate([recv, zeros], axis=1),
                             jnp.concatenate([zeros, recv], axis=1))
            recv = send(near(j) + lead, ring)
        else:
            recv = send(near(j) + recv, ring)
    other = lax.ppermute(
        halves(recv, 1 - core).astype(jnp.bfloat16), "head", [(i, i ^ 1) for i in range(n_head)]
    ).astype(jnp.float32)
    return (halves(recv, core) + other + own_sum).astype(jnp.bfloat16)


def solution(mesh):
    placed = (P("ctx", "head"), P("ctx", "head"), P("ctx", "head"), P(), P("head"), P("head", None))
    n_ctx, n_head = mesh.shape["ctx"], mesh.shape["head"]
    return jax.shard_map(
        lambda *a: local(n_ctx, n_head, *a),
        mesh=mesh,
        in_specs=placed,
        out_specs=P(("ctx", "head"), None),
        check_vma=False,
    )
```

```python
import jax
import jax.numpy as jnp
from jax import lax
from jax.sharding import PartitionSpec as P

DH = 128


def shift_from(x, axis, size, step):
    return lax.ppermute(x, axis, [(i, i + step) for i in range(size - step)])


def local(n_ctx, n_head, queries, keys, values, doc_lengths, norm_gain, w_out):
    tok = queries.shape[0]
    heads_here = queries.shape[1] // DH
    place = lax.axis_index("ctx")
    first = place * tok
    ends = jnp.cumsum(doc_lengths)

    def doc_at(p):
        return jnp.sum((ends <= p).astype(jnp.int32))

    def whole_open(j):
        return ((j > 0) & (doc_at(j * tok - 1) == doc_at(j * tok + tok - 1))).astype(jnp.float32)

    offsets = jnp.arange(tok, dtype=jnp.int32)
    where_now = first + offsets
    doc = jnp.sum((ends[None, :] <= where_now[:, None]).astype(jnp.int32), axis=1)
    continues = (place > 0) & (doc_at(first - 1) == doc[0])
    q_heads = queries.reshape(tok, heads_here, DH)
    k_heads = keys.reshape(tok, heads_here, DH)
    v_heads = values.reshape(tok, heads_here, DH)

    last_doc = doc_at(first + tok - 1)
    last_start = jnp.where(last_doc > 0, ends[jnp.maximum(last_doc - 1, 0)], 0)
    last = where_now >= last_start
    k_last = jnp.where(last[:, None, None], k_heads, jnp.zeros_like(k_heads))
    own = jnp.einsum("thd,the->hde", k_last, v_heads, preferred_element_type=jnp.float32)
    wo1 = whole_open(place - 1)
    wo2 = whole_open(place - 2)
    own_b = own.astype(jnp.bfloat16)
    r1 = shift_from(own_b, "ctx", n_ctx, 1).astype(jnp.float32)
    r2 = shift_from(own_b, "ctx", n_ctx, 2).astype(jnp.float32)
    near = r1 + wo1 * r2
    r3 = shift_from(near.astype(jnp.bfloat16), "ctx", n_ctx, 2).astype(jnp.float32)
    carried = (near + (wo1 * wo2) * r3) * continues.astype(jnp.float32)

    causal = offsets[:, None] >= offsets[None, :]
    allowed = (doc[:, None] == doc[None, :]) & causal
    scores = jnp.einsum("thd,shd->hts", q_heads, k_heads, preferred_element_type=jnp.float32)
    weights = jnp.where(allowed[None], scores, 0.0).astype(jnp.bfloat16)
    intra = jnp.einsum("hts,shd->thd", weights, v_heads, preferred_element_type=jnp.float32)
    active = (continues & (doc == doc[0])).astype(jnp.float32)
    inter = jnp.einsum(
        "thd,hde->the", q_heads.astype(jnp.float32), carried, precision=lax.Precision.HIGHEST
    )
    attn = intra + inter * active[:, None, None]
    meansq = jnp.mean(attn * attn, axis=-1, keepdims=True)
    normed = attn * lax.rsqrt(meansq + 1e-06) * norm_gain.reshape(heads_here, DH)
    hidden = normed.reshape(tok, heads_here * DH).astype(jnp.bfloat16)

    n_chip = n_head // 2
    rows = tok // n_chip
    half_rows = rows // 2
    me = lax.axis_index("head")
    core = me % 2
    chip = me // 2
    dirn = 1 - 2 * core
    by_chip = hidden.reshape(n_chip, rows, hidden.shape[1])

    def take(a, idx):
        return lax.dynamic_index_in_dim(a, idx % n_chip, 0, False)

    def halves(a, which):
        return lax.dynamic_slice_in_dim(a, which * half_rows, half_rows, 0)

    far = chip + n_chip // 2
    steps = n_chip // 2 - 1
    sib_rows = jnp.concatenate(
        [take(by_chip, chip - dirn * j) for j in range(1, steps + 1)]
        + [take(by_chip, far), halves(take(by_chip, chip), 1 - core)],
        axis=0,
    )
    sib_part = jnp.dot(sib_rows, w_out, preferred_element_type=jnp.float32).astype(jnp.bfloat16)
    far_part = sib_part[steps * rows:(steps + 1) * rows]
    to_sib = jnp.concatenate(
        [
            sib_part[:steps * rows],
            halves(far_part, 1 - core),
            sib_part[(steps + 1) * rows:],
        ],
        axis=0,
    )
    from_sib = lax.ppermute(to_sib, "head", [(i, i ^ 1) for i in range(n_head)]).astype(jnp.float32)
    my_rows = jnp.concatenate(
        [take(by_chip, chip + dirn * j) for j in range(1, steps + 1)]
        + [halves(take(by_chip, chip), core)],
        axis=0,
    )
    my_part = lax.optimization_barrier(
        jnp.dot(my_rows, w_out, preferred_element_type=jnp.float32).astype(jnp.bfloat16)
    ).astype(jnp.float32)

    def near(j):
        return my_part[(j - 1) * rows:j * rows] + from_sib[(j - 1) * rows:j * rows]

    far_sum = halves(far_part, core).astype(jnp.float32) + from_sib[
        steps * rows:steps * rows + half_rows
    ]
    own_sum = my_part[steps * rows:] + from_sib[steps * rows + half_rows:]

    ring = [(i, (i + 2) % n_head) if i % 2 == 0 else (i, (i - 2) % n_head) for i in range(n_head)]

    def send(x, perm):
        return lax.ppermute(x.astype(jnp.bfloat16), "head", perm).astype(jnp.float32)

    recv = send(far_sum, ring)
    zeros = jnp.zeros_like(recv)
    for j in range(steps, 0, -1):
        if j == steps:
            lead = jnp.where(core == 0, jnp.concatenate([recv, zeros], axis=0),
                             jnp.concatenate([zeros, recv], axis=0))
            recv = send(near(j) + lead, ring)
        else:
            recv = send(near(j) + recv, ring)
    other = lax.ppermute(
        halves(recv, 1 - core).astype(jnp.bfloat16), "head", [(i, i ^ 1) for i in range(n_head)]
    ).astype(jnp.float32)
    return (halves(recv, core) + other + own_sum).astype(jnp.bfloat16)


def solution(mesh):
    placed = (P("ctx", "head"), P("ctx", "head"), P("ctx", "head"), P(), P("head"), P("head", None))
    n_ctx, n_head = mesh.shape["ctx"], mesh.shape["head"]
    return jax.shard_map(
        lambda *a: local(n_ctx, n_head, *a),
        mesh=mesh,
        in_specs=placed,
        out_specs=P(("ctx", "head"), None),
        check_vma=False,
    )
```

```python
import jax
import jax.numpy as jnp
from jax import lax
from jax.sharding import PartitionSpec as P

DH = 128


def shift_from(x, axis, size, step):
    return lax.ppermute(x, axis, [(i, i + step) for i in range(size - step)])


def local(n_ctx, n_head, queries, keys, values, doc_lengths, norm_gain, w_out):
    tok = queries.shape[0]
    heads_here = queries.shape[1] // DH
    place = lax.axis_index("ctx")
    first = place * tok
    ends = jnp.cumsum(doc_lengths)

    def doc_at(p):
        return jnp.sum((ends <= p).astype(jnp.int32))

    def whole_open(j):
        return ((j > 0) & (doc_at(j * tok - 1) == doc_at(j * tok + tok - 1))).astype(jnp.float32)

    offsets = jnp.arange(tok, dtype=jnp.int32)
    where_now = first + offsets
    doc = jnp.sum((ends[None, :] <= where_now[:, None]).astype(jnp.int32), axis=1)
    continues = (place > 0) & (doc_at(first - 1) == doc[0])
    q_heads = queries.reshape(tok, heads_here, DH)
    k_heads = keys.reshape(tok, heads_here, DH)
    v_heads = values.reshape(tok, heads_here, DH)

    last_doc = doc_at(first + tok - 1)
    last_start = jnp.where(last_doc > 0, ends[jnp.maximum(last_doc - 1, 0)], 0)
    last = where_now >= last_start
    k_last = jnp.where(last[:, None, None], k_heads, jnp.zeros_like(k_heads))
    own = jnp.einsum("thd,the->hde", k_last, v_heads, preferred_element_type=jnp.float32)
    wo1 = whole_open(place - 1)
    wo2 = whole_open(place - 2)
    own_b = own.astype(jnp.bfloat16)
    r1 = shift_from(own_b, "ctx", n_ctx, 1).astype(jnp.float32)
    r2 = shift_from(own_b, "ctx", n_ctx, 2).astype(jnp.float32)
    near = r1 + wo1 * r2
    r3 = shift_from(near.astype(jnp.bfloat16), "ctx", n_ctx, 2).astype(jnp.float32)
    carried = (near + (wo1 * wo2) * r3) * continues.astype(jnp.float32)

    causal = offsets[:, None] >= offsets[None, :]
    allowed = (doc[:, None] == doc[None, :]) & causal
    scores = jnp.einsum("thd,shd->hts", q_heads, k_heads, preferred_element_type=jnp.float32)
    weights = jnp.where(allowed[None], scores, 0.0).astype(jnp.bfloat16)
    intra = jnp.einsum("hts,shd->thd", weights, v_heads, preferred_element_type=jnp.float32)
    active = (continues & (doc == doc[0])).astype(jnp.float32)
    inter = jnp.einsum(
        "thd,hde->the", q_heads.astype(jnp.float32), carried, precision=lax.Precision.HIGHEST
    )
    attn = intra + inter * active[:, None, None]
    meansq = jnp.mean(attn * attn, axis=-1, keepdims=True)
    normed = attn * lax.rsqrt(meansq + 1e-06) * norm_gain.reshape(heads_here, DH)
    hidden = normed.reshape(tok, heads_here * DH).astype(jnp.bfloat16)

    n_chip = n_head // 2
    rows = tok // n_chip
    half_rows = rows // 2
    me = lax.axis_index("head")
    core = me % 2
    chip = me // 2
    dirn = 1 - 2 * core
    by_chip = hidden.reshape(n_chip, rows, hidden.shape[1])

    def take(a, idx):
        return lax.dynamic_index_in_dim(a, idx % n_chip, 0, False)

    def halves(a, which):
        return lax.dynamic_slice_in_dim(a, which * half_rows, half_rows, 0)

    far = chip + n_chip // 2
    steps = n_chip // 2 - 1
    pair = [(i, i ^ 1) for i in range(n_head)]
    far_part = jnp.dot(take(by_chip, far), w_out, preferred_element_type=jnp.float32).astype(jnp.bfloat16)
    far_sib = lax.ppermute(halves(far_part, 1 - core), "head", pair)
    far_sum = halves(far_part, core).astype(jnp.float32) + far_sib.astype(jnp.float32)
    sib_rows = jnp.concatenate(
        [take(by_chip, chip - dirn * j) for j in range(1, steps + 1)]
        + [halves(take(by_chip, chip), 1 - core)],
        axis=0,
    )
    to_sib = jnp.dot(sib_rows, w_out, preferred_element_type=jnp.float32).astype(jnp.bfloat16)
    from_sib = lax.ppermute(to_sib, "head", pair).astype(jnp.float32)
    my_rows = jnp.concatenate(
        [take(by_chip, chip + dirn * j) for j in range(1, steps + 1)]
        + [halves(take(by_chip, chip), core)],
        axis=0,
    )
    my_part = lax.optimization_barrier(
        jnp.dot(my_rows, w_out, preferred_element_type=jnp.float32).astype(jnp.bfloat16)
    ).astype(jnp.float32)

    def near(j):
        return my_part[(j - 1) * rows:j * rows] + from_sib[(j - 1) * rows:j * rows]

    own_sum = my_part[steps * rows:] + from_sib[steps * rows:]

    ring = [(i, (i + 2) % n_head) if i % 2 == 0 else (i, (i - 2) % n_head) for i in range(n_head)]

    def send(x, perm):
        return lax.ppermute(x.astype(jnp.bfloat16), "head", perm).astype(jnp.float32)

    recv = send(far_sum, ring)
    zeros = jnp.zeros_like(recv)
    for j in range(steps, 0, -1):
        if j == steps:
            lead = jnp.where(core == 0, jnp.concatenate([recv, zeros], axis=0),
                             jnp.concatenate([zeros, recv], axis=0))
            recv = send(near(j) + lead, ring)
        else:
            recv = send(near(j) + recv, ring)
    other = lax.ppermute(halves(recv, 1 - core).astype(jnp.bfloat16), "head", pair).astype(jnp.float32)
    return (halves(recv, core) + other + own_sum).astype(jnp.bfloat16)


def solution(mesh):
    placed = (P("ctx", "head"), P("ctx", "head"), P("ctx", "head"), P(), P("head"), P("head", None))
    n_ctx, n_head = mesh.shape["ctx"], mesh.shape["head"]
    return jax.shard_map(
        lambda *a: local(n_ctx, n_head, *a),
        mesh=mesh,
        in_specs=placed,
        out_specs=P(("ctx", "head"), None),
        check_vma=False,
    )
```

```python
import jax
import jax.numpy as jnp
from jax import lax
from jax.sharding import PartitionSpec as P

DH = 128


def shift_from(x, axis, size, step):
    return lax.ppermute(x, axis, [(i, i + step) for i in range(size - step)])


def local(n_ctx, n_head, queries, keys, values, doc_lengths, norm_gain, w_out):
    tok = queries.shape[0]
    heads_here = queries.shape[1] // DH
    place = lax.axis_index("ctx")
    first = place * tok
    ends = jnp.cumsum(doc_lengths)

    def doc_at(p):
        return jnp.sum((ends <= p).astype(jnp.int32))

    def whole_open(j):
        return ((j > 0) & (doc_at(j * tok - 1) == doc_at(j * tok + tok - 1))).astype(jnp.float32)

    offsets = jnp.arange(tok, dtype=jnp.int32)
    where_now = first + offsets
    doc = jnp.sum((ends[None, :] <= where_now[:, None]).astype(jnp.int32), axis=1)
    continues = (place > 0) & (doc_at(first - 1) == doc[0])
    q_heads = queries.reshape(tok, heads_here, DH)
    k_heads = keys.reshape(tok, heads_here, DH)
    v_heads = values.reshape(tok, heads_here, DH)

    last_doc = doc_at(first + tok - 1)
    last_start = jnp.where(last_doc > 0, ends[jnp.maximum(last_doc - 1, 0)], 0)
    last = where_now >= last_start
    k_last = jnp.where(last[:, None, None], k_heads, jnp.zeros_like(k_heads))
    own = jnp.einsum("thd,the->hde", k_last, v_heads, preferred_element_type=jnp.float32)
    wo1 = whole_open(place - 1)
    wo2 = whole_open(place - 2)
    own_b = own.astype(jnp.bfloat16)
    r1 = shift_from(own_b, "ctx", n_ctx, 1).astype(jnp.float32)
    r2 = shift_from(own_b, "ctx", n_ctx, 2).astype(jnp.float32)
    near = r1 + wo1 * r2
    r3 = shift_from(near.astype(jnp.bfloat16), "ctx", n_ctx, 2).astype(jnp.float32)
    carried = (near + (wo1 * wo2) * r3) * continues.astype(jnp.float32)

    causal = offsets[:, None] >= offsets[None, :]
    allowed = (doc[:, None] == doc[None, :]) & causal
    scores = jnp.einsum("thd,shd->hts", q_heads, k_heads, preferred_element_type=jnp.float32)
    weights = jnp.where(allowed[None], scores, 0.0).astype(jnp.bfloat16)
    intra = jnp.einsum("hts,shd->thd", weights, v_heads, preferred_element_type=jnp.float32)
    active = (continues & (doc == doc[0])).astype(jnp.float32)
    inter = jnp.einsum(
        "thd,hde->the", q_heads.astype(jnp.float32), carried, precision=lax.Precision.HIGHEST
    )
    attn = intra + inter * active[:, None, None]
    meansq = jnp.mean(attn * attn, axis=-1, keepdims=True)
    normed = attn * lax.rsqrt(meansq + 1e-06) * norm_gain.reshape(heads_here, DH)
    hidden = normed.reshape(tok, heads_here * DH).astype(jnp.bfloat16)

    n_chip = n_head // 2
    rows = tok // n_chip
    half_rows = rows // 2
    me = lax.axis_index("head")
    core = me % 2
    chip = me // 2
    dirn = 1 - 2 * core
    by_chip = hidden.reshape(n_chip, rows, hidden.shape[1])

    def take(a, idx):
        return lax.dynamic_index_in_dim(a, idx % n_chip, 0, False)

    def halves(a, which):
        return lax.dynamic_slice_in_dim(a, which * half_rows, half_rows, 0)

    far = chip + n_chip // 2
    steps = n_chip // 2 - 1
    pair = [(i, i ^ 1) for i in range(n_head)]
    far_part = lax.dot_general(
        w_out, take(by_chip, far), (((0,), (1,)), ((), ())), preferred_element_type=jnp.float32
    ).astype(jnp.bfloat16).T
    far_sib = lax.ppermute(halves(far_part, 1 - core), "head", pair)
    far_sum = halves(far_part, core).astype(jnp.float32) + far_sib.astype(jnp.float32)
    sib_rows = jnp.concatenate(
        [take(by_chip, chip - dirn * j) for j in range(1, steps + 1)]
        + [halves(take(by_chip, chip), 1 - core)],
        axis=0,
    )
    to_sib = jnp.dot(sib_rows, w_out, preferred_element_type=jnp.float32).astype(jnp.bfloat16)
    from_sib = lax.ppermute(to_sib, "head", pair).astype(jnp.float32)
    my_rows = jnp.concatenate(
        [take(by_chip, chip + dirn * j) for j in range(1, steps + 1)]
        + [halves(take(by_chip, chip), core)],
        axis=0,
    )
    my_part = lax.optimization_barrier(
        jnp.dot(my_rows, w_out, preferred_element_type=jnp.float32).astype(jnp.bfloat16)
    ).astype(jnp.float32)

    def near(j):
        return my_part[(j - 1) * rows:j * rows] + from_sib[(j - 1) * rows:j * rows]

    own_sum = my_part[steps * rows:] + from_sib[steps * rows:]

    ring = [(i, (i + 2) % n_head) if i % 2 == 0 else (i, (i - 2) % n_head) for i in range(n_head)]

    def send(x, perm):
        return lax.ppermute(x.astype(jnp.bfloat16), "head", perm).astype(jnp.float32)

    recv = send(far_sum, ring)
    zeros = jnp.zeros_like(recv)
    for j in range(steps, 1, -1):
        if j == steps:
            lead = jnp.where(core == 0, jnp.concatenate([recv, zeros], axis=0),
                             jnp.concatenate([zeros, recv], axis=0))
            recv = send(near(j) + lead, ring)
        else:
            recv = send(near(j) + recv, ring)
    last = near(1) + recv
    cross = [(i, (i + 3) % n_head) if i % 2 == 0 else (i, (i - 3) % n_head) for i in range(n_head)]
    same = send(halves(last, core), ring)
    other = send(halves(last, 1 - core), cross)
    return (same + other + own_sum).astype(jnp.bfloat16)


def solution(mesh):
    placed = (P("ctx", "head"), P("ctx", "head"), P("ctx", "head"), P(), P("head"), P("head", None))
    n_ctx, n_head = mesh.shape["ctx"], mesh.shape["head"]
    return jax.shard_map(
        lambda *a: local(n_ctx, n_head, *a),
        mesh=mesh,
        in_specs=placed,
        out_specs=P(("ctx", "head"), None),
        check_vma=False,
    )
```

```python
import jax
import jax.numpy as jnp
from jax import lax
from jax.sharding import PartitionSpec as P


DH = 128


def shift_from(x, axis, size, step):
    return lax.ppermute(x, axis, [(i, i + step) for i in range(size - step)])


def local(n_ctx, n_head, queries, keys, values, doc_lengths, norm_gain, w_out):
    tok = queries.shape[0]
    heads_here = queries.shape[1] // DH
    place = lax.axis_index("ctx")
    first = place * tok
    ends = jnp.cumsum(doc_lengths.reshape(1, -1), axis=1).reshape(-1)

    def doc_at(p):
        return jnp.sum((ends <= p).astype(jnp.int32))

    def whole_open(j):
        return ((j > 0) & (doc_at(j * tok - 1) == doc_at(j * tok + tok - 1))).astype(jnp.float32)

    offsets = jnp.arange(tok, dtype=jnp.int32)
    where_now = first + offsets
    doc = jnp.sum((ends[None, :] <= where_now[:, None]).astype(jnp.int32), axis=1)
    continues = (place > 0) & (doc_at(first - 1) == doc[0])
    q_heads = queries.reshape(tok, heads_here, DH)
    k_heads = keys.reshape(tok, heads_here, DH)
    v_heads = values.reshape(tok, heads_here, DH)

    last_doc = doc_at(first + tok - 1)
    last_start = jnp.where(last_doc > 0, ends[jnp.maximum(last_doc - 1, 0)], 0)
    last = where_now >= last_start
    k_last = jnp.where(last[:, None, None], k_heads, jnp.zeros_like(k_heads))
    own = jnp.einsum("thd,the->hde", k_last, v_heads, preferred_element_type=jnp.float32)
    wo1 = whole_open(place - 1)
    wo2 = whole_open(place - 2)
    own_b = own.astype(jnp.bfloat16)
    r1 = shift_from(own_b, "ctx", n_ctx, 1).astype(jnp.float32)
    r2 = shift_from(own_b, "ctx", n_ctx, 2).astype(jnp.float32)
    near = r1 + wo1 * r2
    r3 = shift_from(near.astype(jnp.bfloat16), "ctx", n_ctx, 2).astype(jnp.float32)
    carried = (near + (wo1 * wo2) * r3) * continues.astype(jnp.float32)

    causal = offsets[:, None] >= offsets[None, :]
    allowed = (doc[:, None] == doc[None, :]) & causal
    scores = jnp.einsum("thd,shd->hts", q_heads, k_heads, preferred_element_type=jnp.float32)
    weights = jnp.where(allowed[None], scores, 0.0).astype(jnp.bfloat16)
    intra = jnp.einsum("hts,shd->thd", weights, v_heads, preferred_element_type=jnp.float32)
    active = (continues & (doc == doc[0])).astype(jnp.float32)
    inter = jnp.einsum(
        "thd,hde->the", q_heads.astype(jnp.float32), carried, precision=lax.Precision.HIGHEST
    )
    attn = intra + inter * active[:, None, None]
    meansq = jnp.mean(attn * attn, axis=-1, keepdims=True)
    normed = attn * lax.rsqrt(meansq + 1e-06) * norm_gain.reshape(heads_here, DH)
    hidden = normed.reshape(tok, heads_here * DH).astype(jnp.bfloat16)

    n_chip = n_head // 2
    rows = tok // n_chip
    half_rows = rows // 2
    me = lax.axis_index("head")
    core = me % 2
    chip = me // 2
    dirn = 1 - 2 * core
    by_chip = hidden.reshape(n_chip, rows, hidden.shape[1])

    def take(a, idx):
        return lax.dynamic_index_in_dim(a, idx % n_chip, 0, False)

    def halves(a, which):
        return lax.dynamic_slice_in_dim(a, which * half_rows, half_rows, 0)

    far = chip + n_chip // 2
    steps = n_chip // 2 - 1
    pair = [(i, i ^ 1) for i in range(n_head)]
    far_part = lax.dot_general(
        w_out, take(by_chip, far), (((0,), (1,)), ((), ())), preferred_element_type=jnp.float32
    ).astype(jnp.bfloat16).T
    far_sib = lax.ppermute(halves(far_part, 1 - core), "head", pair)
    far_sum = halves(far_part, core).astype(jnp.float32) + far_sib.astype(jnp.float32)
    sib_rows = jnp.concatenate(
        [take(by_chip, chip - dirn * j) for j in range(1, steps + 1)]
        + [halves(take(by_chip, chip), 1 - core)],
        axis=0,
    )
    to_sib = jnp.dot(sib_rows, w_out, preferred_element_type=jnp.float32).astype(jnp.bfloat16)
    from_sib = lax.ppermute(to_sib, "head", pair).astype(jnp.float32)
    my_rows = jnp.concatenate(
        [take(by_chip, chip + dirn * j) for j in range(1, steps + 1)]
        + [halves(take(by_chip, chip), core)],
        axis=0,
    )
    my_part = lax.optimization_barrier(
        jnp.dot(my_rows, w_out, preferred_element_type=jnp.float32).astype(jnp.bfloat16)
    ).astype(jnp.float32)

    def near(j):
        return my_part[(j - 1) * rows:j * rows] + from_sib[(j - 1) * rows:j * rows]

    own_sum = my_part[steps * rows:] + from_sib[steps * rows:]

    ring = [(i, (i + 2) % n_head) if i % 2 == 0 else (i, (i - 2) % n_head) for i in range(n_head)]

    def send(x, perm):
        return lax.ppermute(x.astype(jnp.bfloat16), "head", perm).astype(jnp.float32)

    recv = send(far_sum, ring)
    zeros = jnp.zeros_like(recv)
    for j in range(steps, 1, -1):
        if j == steps:
            lead = jnp.where(core == 0, jnp.concatenate([recv, zeros], axis=0),
                             jnp.concatenate([zeros, recv], axis=0))
            recv = send(near(j) + lead, ring)
        else:
            recv = send(near(j) + recv, ring)
    last = near(1) + recv
    cross = [(i, (i + 3) % n_head) if i % 2 == 0 else (i, (i - 3) % n_head) for i in range(n_head)]
    same = send(halves(last, core), ring)
    other = send(halves(last, 1 - core), cross)
    return (same + other + own_sum).astype(jnp.bfloat16)


def solution(mesh):
    placed = (P("ctx", "head"), P("ctx", "head"), P("ctx", "head"), P(), P("head"), P("head", None))
    n_ctx, n_head = mesh.shape["ctx"], mesh.shape["head"]

    def body(*a):
        return local(n_ctx, n_head, *a)

    return jax.shard_map(
        body,
        mesh=mesh,
        in_specs=placed,
        out_specs=P(("ctx", "head"), None),
        check_vma=False,
    )
```

```python
import jax
import jax.numpy as jnp
from jax import lax
from jax.sharding import PartitionSpec as P


DH = 128


def shift_from(x, axis, size, step):
    return lax.ppermute(x, axis, [(i, i + step) for i in range(size - step)])


def local(n_ctx, n_head, queries, keys, values, doc_lengths, norm_gain, w_out):
    tok = queries.shape[0]
    heads_here = queries.shape[1] // DH
    place = lax.axis_index("ctx")
    first = place * tok
    ends = jnp.cumsum(doc_lengths.reshape(1, -1), axis=1).reshape(-1)

    def doc_at(p):
        return jnp.sum((ends <= p).astype(jnp.int32))

    def whole_open(j):
        return ((j > 0) & (doc_at(j * tok - 1) == doc_at(j * tok + tok - 1))).astype(jnp.float32)

    offsets = jnp.arange(tok, dtype=jnp.int32)
    where_now = first + offsets
    doc = jnp.sum((ends[None, :] <= where_now[:, None]).astype(jnp.int32), axis=1)
    continues = (place > 0) & (doc_at(first - 1) == doc[0])
    q_heads = queries.reshape(tok, heads_here, DH)
    k_heads = keys.reshape(tok, heads_here, DH)
    v_heads = values.reshape(tok, heads_here, DH)

    last_doc = doc_at(first + tok - 1)
    last_start = jnp.where(last_doc > 0, ends[jnp.maximum(last_doc - 1, 0)], 0)
    last = where_now >= last_start
    k_last = jnp.where(last[:, None, None], k_heads, jnp.zeros_like(k_heads))
    own = jnp.einsum("thd,the->hde", k_last, v_heads, preferred_element_type=jnp.float32)
    wo1 = whole_open(place - 1)
    wo2 = whole_open(place - 2)
    own_b = own.astype(jnp.bfloat16)
    r1 = shift_from(own_b, "ctx", n_ctx, 1).astype(jnp.float32)
    r2 = shift_from(own_b, "ctx", n_ctx, 2).astype(jnp.float32)
    near = r1 + wo1 * r2
    r3 = shift_from(near.astype(jnp.bfloat16), "ctx", n_ctx, 2).astype(jnp.float32)
    carried = (near + (wo1 * wo2) * r3) * continues.astype(jnp.float32)

    causal = offsets[:, None] >= offsets[None, :]
    allowed = (doc[:, None] == doc[None, :]) & causal
    scores = jnp.einsum("thd,shd->hts", q_heads, k_heads, preferred_element_type=jnp.float32)
    weights = jnp.where(allowed[None], scores, 0.0).astype(jnp.bfloat16)
    intra = jnp.einsum("hts,shd->thd", weights, v_heads, preferred_element_type=jnp.float32)
    active = (continues & (doc == doc[0])).astype(jnp.float32)
    inter = jnp.einsum(
        "thd,hde->the", q_heads.astype(jnp.float32), carried, precision=lax.Precision.HIGHEST
    )
    attn = intra + inter * active[:, None, None]
    meansq = jnp.mean(attn * attn, axis=-1, keepdims=True)
    normed = attn * lax.rsqrt(meansq + 1e-06) * norm_gain.reshape(heads_here, DH)
    hidden = normed.reshape(tok, heads_here * DH).astype(jnp.bfloat16)

    n_chip = n_head // 2
    rows = tok // n_chip
    half_rows = rows // 2
    me = lax.axis_index("head")
    core = me % 2
    chip = me // 2
    dirn = 1 - 2 * core
    by_chip = hidden.reshape(n_chip, rows, hidden.shape[1])

    def take(a, idx):
        return lax.dynamic_index_in_dim(a, idx % n_chip, 0, False)

    def halves(a, which):
        return lax.dynamic_slice_in_dim(a, which * half_rows, half_rows, 0)

    far = chip + n_chip // 2
    steps = n_chip // 2 - 1
    pair = [(i, i ^ 1) for i in range(n_head)]
    first_rows = jnp.concatenate(
        [take(by_chip, far), take(by_chip, chip - dirn * steps), take(by_chip, chip + dirn * steps)],
        axis=0,
    )
    first_part = jnp.dot(first_rows, w_out, preferred_element_type=jnp.float32).astype(jnp.bfloat16)
    far_part = first_part[:rows]
    to_sib_first = jnp.concatenate([halves(far_part, 1 - core), first_part[rows:2 * rows]], axis=0)
    from_sib_first = lax.ppermute(to_sib_first, "head", pair).astype(jnp.float32)
    far_sum = halves(far_part, core).astype(jnp.float32) + from_sib_first[:half_rows]
    near_last = first_part[2 * rows:].astype(jnp.float32) + from_sib_first[half_rows:]
    sib_rows = jnp.concatenate(
        [take(by_chip, chip - dirn * j) for j in range(1, steps)]
        + [halves(take(by_chip, chip), 1 - core)],
        axis=0,
    )
    to_sib = jnp.dot(sib_rows, w_out, preferred_element_type=jnp.float32).astype(jnp.bfloat16)
    from_sib = lax.ppermute(to_sib, "head", pair).astype(jnp.float32)
    my_rows = jnp.concatenate(
        [take(by_chip, chip + dirn * j) for j in range(1, steps)]
        + [halves(take(by_chip, chip), core)],
        axis=0,
    )
    my_part = lax.optimization_barrier(
        jnp.dot(my_rows, w_out, preferred_element_type=jnp.float32).astype(jnp.bfloat16)
    ).astype(jnp.float32)

    def near(j):
        if j == steps:
            return near_last
        return my_part[(j - 1) * rows:j * rows] + from_sib[(j - 1) * rows:j * rows]

    own_sum = my_part[(steps - 1) * rows:] + from_sib[(steps - 1) * rows:]

    ring = [(i, (i + 2) % n_head) if i % 2 == 0 else (i, (i - 2) % n_head) for i in range(n_head)]

    def send(x, perm):
        return lax.ppermute(x.astype(jnp.bfloat16), "head", perm).astype(jnp.float32)

    recv = send(far_sum, ring)
    zeros = jnp.zeros_like(recv)
    for j in range(steps, 1, -1):
        if j == steps:
            lead = jnp.where(core == 0, jnp.concatenate([recv, zeros], axis=0),
                             jnp.concatenate([zeros, recv], axis=0))
            recv = send(near(j) + lead, ring)
        else:
            recv = send(near(j) + recv, ring)
    last = near(1) + recv
    cross = [(i, (i + 3) % n_head) if i % 2 == 0 else (i, (i - 3) % n_head) for i in range(n_head)]
    same = send(halves(last, core), ring)
    other = send(halves(last, 1 - core), cross)
    return (same + other + own_sum).astype(jnp.bfloat16)


def solution(mesh):
    placed = (P("ctx", "head"), P("ctx", "head"), P("ctx", "head"), P(), P("head"), P("head", None))
    n_ctx, n_head = mesh.shape["ctx"], mesh.shape["head"]

    def body(*a):
        return local(n_ctx, n_head, *a)

    return jax.shard_map(
        body,
        mesh=mesh,
        in_specs=placed,
        out_specs=P(("ctx", "head"), None),
        check_vma=False,
    )
```

```python
import jax
import jax.numpy as jnp
from jax import lax
from jax.sharding import PartitionSpec as P


DH = 128


def shift_from(x, axis, size, step):
    return lax.ppermute(x, axis, [(i, i + step) for i in range(size - step)])


def local(n_ctx, n_head, queries, keys, values, doc_lengths, norm_gain, w_out):
    tok = queries.shape[0]
    heads_here = queries.shape[1] // DH
    place = lax.axis_index("ctx")
    first = place * tok
    ends = jnp.cumsum(doc_lengths.reshape(1, -1), axis=1).reshape(-1)

    def doc_at(p):
        return jnp.sum((ends <= p).astype(jnp.int32))

    def whole_open(j):
        return ((j > 0) & (doc_at(j * tok - 1) == doc_at(j * tok + tok - 1))).astype(jnp.float32)

    offsets = jnp.arange(tok, dtype=jnp.int32)
    where_now = first + offsets
    doc = jnp.sum((ends[None, :] <= where_now[:, None]).astype(jnp.int32), axis=1)
    continues = (place > 0) & (doc_at(first - 1) == doc[0])
    q_heads = queries.reshape(tok, heads_here, DH)
    k_heads = keys.reshape(tok, heads_here, DH)
    v_heads = values.reshape(tok, heads_here, DH)

    last_doc = doc_at(first + tok - 1)
    last_start = jnp.where(last_doc > 0, ends[jnp.maximum(last_doc - 1, 0)], 0)
    last = where_now >= last_start
    k_last = jnp.where(last[:, None, None], k_heads, jnp.zeros_like(k_heads))
    own = jnp.einsum("thd,the->hde", k_last, v_heads, preferred_element_type=jnp.float32)
    wo1 = whole_open(place - 1)
    wo2 = whole_open(place - 2)
    own_b = own.astype(jnp.bfloat16)
    r1 = shift_from(own_b, "ctx", n_ctx, 1).astype(jnp.float32)
    r2 = shift_from(own_b, "ctx", n_ctx, 2).astype(jnp.float32)
    near = r1 + wo1 * r2
    r3 = shift_from(near.astype(jnp.bfloat16), "ctx", n_ctx, 2).astype(jnp.float32)
    carried = (near + (wo1 * wo2) * r3) * continues.astype(jnp.float32)

    causal = offsets[:, None] >= offsets[None, :]
    allowed = (doc[:, None] == doc[None, :]) & causal
    scores = jnp.einsum("thd,shd->hts", q_heads, k_heads, preferred_element_type=jnp.float32)
    weights = jnp.where(allowed[None], scores, 0.0).astype(jnp.bfloat16)
    intra = jnp.einsum("hts,shd->thd", weights, v_heads, preferred_element_type=jnp.float32)
    active = (continues & (doc == doc[0])).astype(jnp.float32)
    inter = jnp.einsum(
        "thd,hde->the", q_heads.astype(jnp.float32), carried, precision=lax.Precision.HIGHEST
    )
    attn = intra + inter * active[:, None, None]
    meansq = jnp.mean(attn * attn, axis=-1, keepdims=True)
    normed = attn * lax.rsqrt(meansq + 1e-06) * norm_gain.reshape(heads_here, DH)
    hidden = normed.reshape(tok, heads_here * DH).astype(jnp.bfloat16)

    n_chip = n_head // 2
    rows = tok // n_chip
    half_rows = rows // 2
    me = lax.axis_index("head")
    core = me % 2
    chip = me // 2
    dirn = 1 - 2 * core
    by_chip = hidden.reshape(n_chip, rows, hidden.shape[1])

    def take(a, idx):
        return lax.dynamic_index_in_dim(a, idx % n_chip, 0, False)

    def halves(a, which):
        return lax.dynamic_slice_in_dim(a, which * half_rows, half_rows, 0)

    far = chip + n_chip // 2
    steps = n_chip // 2 - 1
    pair = [(i, i ^ 1) for i in range(n_head)]
    first_rows = jnp.concatenate(
        [
            halves(take(by_chip, far), 1 - core),
            take(by_chip, chip - dirn * steps),
            halves(take(by_chip, far), core),
            take(by_chip, chip + dirn * steps),
        ],
        axis=0,
    )
    first_part = jnp.dot(first_rows, w_out, preferred_element_type=jnp.float32).astype(jnp.bfloat16)
    lead_rows = half_rows + rows
    from_sib_first = lax.ppermute(first_part[:lead_rows], "head", pair)
    far_sum = (
        first_part[lead_rows:lead_rows + half_rows].astype(jnp.float32)
        + from_sib_first[:half_rows].astype(jnp.float32)
    )
    near_last = (
        first_part[lead_rows + half_rows:].astype(jnp.float32)
        + from_sib_first[half_rows:].astype(jnp.float32)
    )
    sib_rows = jnp.concatenate(
        [take(by_chip, chip - dirn * j) for j in range(1, steps)]
        + [halves(take(by_chip, chip), 1 - core)],
        axis=0,
    )
    to_sib = jnp.dot(sib_rows, w_out, preferred_element_type=jnp.float32).astype(jnp.bfloat16)
    from_sib = lax.ppermute(to_sib, "head", pair).astype(jnp.float32)
    my_rows = jnp.concatenate(
        [take(by_chip, chip + dirn * j) for j in range(1, steps)]
        + [halves(take(by_chip, chip), core)],
        axis=0,
    )
    my_part = lax.optimization_barrier(
        jnp.dot(my_rows, w_out, preferred_element_type=jnp.float32).astype(jnp.bfloat16)
    ).astype(jnp.float32)

    def near(j):
        if j == steps:
            return near_last
        return my_part[(j - 1) * rows:j * rows] + from_sib[(j - 1) * rows:j * rows]

    own_sum = my_part[(steps - 1) * rows:] + from_sib[(steps - 1) * rows:]

    ring = [(i, (i + 2) % n_head) if i % 2 == 0 else (i, (i - 2) % n_head) for i in range(n_head)]

    def send(x, perm):
        return lax.ppermute(x.astype(jnp.bfloat16), "head", perm).astype(jnp.float32)

    recv = send(far_sum, ring)
    zeros = jnp.zeros_like(recv)
    for j in range(steps, 1, -1):
        if j == steps:
            lead = jnp.where(core == 0, jnp.concatenate([recv, zeros], axis=0),
                             jnp.concatenate([zeros, recv], axis=0))
            recv = send(near(j) + lead, ring)
        else:
            recv = send(near(j) + recv, ring)
    last = near(1) + recv
    cross = [(i, (i + 3) % n_head) if i % 2 == 0 else (i, (i - 3) % n_head) for i in range(n_head)]
    same = send(halves(last, core), ring)
    other = send(halves(last, 1 - core), cross)
    return (same + other + own_sum).astype(jnp.bfloat16)


def solution(mesh):
    placed = (P("ctx", "head"), P("ctx", "head"), P("ctx", "head"), P(), P("head"), P("head", None))
    n_ctx, n_head = mesh.shape["ctx"], mesh.shape["head"]

    def body(*a):
        return local(n_ctx, n_head, *a)

    return jax.shard_map(
        body,
        mesh=mesh,
        in_specs=placed,
        out_specs=P(("ctx", "head"), None),
        check_vma=False,
    )
```
